256 devices in a mesh: rep: 8 (over z), shard: 32 (over y, x, core).
Axes of the slice: x: 4, y: 4, z: 8, core: 2. Of those that a mesh axis runs over, the one named last changes fastest.
Arguments:
- grad_joined: bfloat16 [8, 1024, 3072], P('rep', 'shard')
- error_joined: float32 [8, 1024, 3072], P('rep', 'shard'), may hold values from -6 to 6
- moment_joined: float32 [1024, 3072], P('shard'), may hold values from -6 to 6
- weight_joined: float32 [1024, 3072], P('shard'), may hold values from -0.1875 to 0.1875
- factor_joined: float32 [32, 3072], replicated, may hold values from -6 to 6
- grad_dense: bfloat16 [8, 1024, 1024], P('rep', 'shard')
- error_dense: float32 [8, 1024, 1024], P('rep', 'shard'), may hold values from -6 to 6
- moment_dense: float32 [1024, 1024], P('shard'), may hold values from -6 to 6
- weight_dense: float32 [1024, 1024], P('shard'), may hold values from -0.1875 to 0.1875
- factor_dense: float32 [32, 1024], replicated, may hold values from -6 to 6
- grad_expand: bfloat16 [8, 1024, 4096], P('rep', 'shard')
- error_expand: float32 [8, 1024, 4096], P('rep', 'shard'), may hold values from -6 to 6
- moment_expand: float32 [1024, 4096], P('shard'), may hold values from -6 to 6
- weight_expand: float32 [1024, 4096], P('shard'), may hold values from -0.1875 to 0.1875
- factor_expand: float32 [32, 4096], replicated, may hold values from -6 to 6
- grad_shrink: bfloat16 [8, 4096, 1024], P('rep', 'shard')
- error_shrink: float32 [8, 4096, 1024], P('rep', 'shard'), may hold values from -6 to 6
- moment_shrink: float32 [4096, 1024], P('shard'), may hold values from -6 to 6
- weight_shrink: float32 [4096, 1024], P('shard'), may hold values from -0.09375 to 0.09375
- factor_shrink: float32 [32, 1024], replicated, may hold values from -6 to 6
- vector_grad: bfloat16 [8, 13312], P('rep', 'shard'), may hold values from -6 to 6
- vector_moment: float32 [13312], P('shard'), may hold values from -6 to 6
- vector_weight: float32 [13312], P('shard'), may hold values from -1.5 to 1.5
Outputs:
- errors_joined: float32 [8, 1024, 3072], P('rep', 'shard')
- moments_joined: float32 [1024, 3072], P('shard')
- weights_joined: float32 [1024, 3072], P('shard')
- factors_joined: float32 [32, 3072], replicated
- errors_dense: float32 [8, 1024, 1024], P('rep', 'shard')
- moments_dense: float32 [1024, 1024], P('shard')
- weights_dense: float32 [1024, 1024], P('shard')
- factors_dense: float32 [32, 1024], replicated
- errors_expand: float32 [8, 1024, 4096], P('rep', 'shard')
- moments_expand: float32 [1024, 4096], P('shard')
- weights_expand: float32 [1024, 4096], P('shard')
- factors_expand: float32 [32, 4096], replicated
- errors_shrink: float32 [8, 4096, 1024], P('rep', 'shard')
- moments_shrink: float32 [4096, 1024], P('shard')
- weights_shrink: float32 [4096, 1024], P('shard')
- factors_shrink: float32 [32, 1024], replicated
- vector_moments: float32 [13312], P('shard')
- vector_weights: float32 [13312], P('shard')
The draws below stay inside these ranges and needn't reach their ends.
All inputs are finite; a program needn't handle non-finite values.
Results may differ from the reference program's by a relative error of at most 0.0003.
Values sent between devices are 32-bit elements; how exact they have to be, the bound alone decides.
No kernel may reach another device: no remote copies, remote signals or barrier semaphores. Data moves between devices by JAX's collectives and lax.ppermute only.
A program may use at most 128 MiB of HBM per device.

```python
import math
import jax
import jax.numpy as jnp
from jax import lax

D = 1024
FF = 4096
RANK = 32
ROUNDS = 2
REPS = 8
VEC = 13312


def gradient_draw(key, height, breadth):
    keys = jax.random.split(key, 4)
    common = jax.random.normal(keys[0], (height, breadth), jnp.float32)
    single = jax.random.normal(keys[1], (REPS, height, breadth), jnp.float32)
    column_scale = jnp.exp(jax.random.uniform(keys[3], (breadth,), jnp.float32, -math.log(2.0), math.log(2.0)))
    mixed = 0.6 * common[None] + 0.8 * single
    ramp = jnp.exp(math.log(3.0) * jnp.arange(height, dtype=jnp.float32) / height)
    rough = jnp.exp(jax.random.uniform(keys[2], (height,), jnp.float32, 0.0, math.log(4.0)))
    row_scale = 0.3 * ramp * rough
    values = mixed * row_scale[None, :, None] * column_scale[None, None, :]
    return values.astype(jnp.bfloat16)


def draw_grad_joined(key, part):
    return gradient_draw(jax.random.fold_in(key, 11), D, 3 * D)


def draw_grad_dense(key, part):
    return gradient_draw(jax.random.fold_in(key, 23), D, D)


def draw_grad_expand(key, part):
    return gradient_draw(jax.random.fold_in(key, 37), D, FF)


def draw_grad_shrink(key, part):
    return gradient_draw(jax.random.fold_in(key, 41), FF, D)


def block_levels(rng, dims, pieces, low, high):
    loudness, own = 1.0, jax.random.fold_in(rng, 6)
    for dim, parts in pieces:
        heights = jnp.exp(jax.random.uniform(jax.random.fold_in(own, dim), (parts,), jnp.float32, low / len(pieces), high / len(pieces)))
        loudness = loudness * jnp.repeat(heights, dims[dim] // parts).reshape([-1 if axis == dim else 1 for axis in range(len(dims))])
    return loudness


def normal_values(key, shape, scale, most, cuts=(), held_as=jnp.bfloat16):
    gain = block_levels(key, shape, cuts, -0.22, 0.18) if cuts else 1.0
    values = jax.random.normal(key, shape, jnp.float32) * scale * gain
    return jnp.minimum(jnp.maximum(values, -most), most).astype(held_as)


def setup_inputs(seed: int = 0) -> dict:
    seeds = jax.random.split(jax.random.key(seed), 24)
    return {
        "grad_joined": draw_grad_joined(jax.random.fold_in(seeds[23], 71), 0),
        "error_joined": normal_values(seeds[1], (REPS, D, 3 * D), 0.5, 6.0, ((0, 8), (1, 32)), jnp.float32),
        "moment_joined": normal_values(seeds[2], (D, 3 * D), 0.5, 6.0, ((0, 32),), jnp.float32),
        "weight_joined": normal_values(seeds[3], (D, 3 * D), D ** -0.5, 0.1875, ((0, 32),), jnp.float32),
        "factor_joined": normal_values(seeds[4], (RANK, 3 * D), 1.0, 6.0, (), jnp.float32),
        "grad_dense": draw_grad_dense(jax.random.fold_in(seeds[23], 71), 0),
        "error_dense": normal_values(seeds[6], (REPS, D, D), 0.5, 6.0, ((0, 8), (1, 32)), jnp.float32),
        "moment_dense": normal_values(seeds[7], (D, D), 0.5, 6.0, ((0, 32),), jnp.float32),
        "weight_dense": normal_values(seeds[8], (D, D), D ** -0.5, 0.1875, ((0, 32),), jnp.float32),
        "factor_dense": normal_values(seeds[9], (RANK, D), 1.0, 6.0, (), jnp.float32),
        "grad_expand": draw_grad_expand(jax.random.fold_in(seeds[23], 71), 0),
        "error_expand": normal_values(seeds[11], (REPS, D, FF), 0.5, 6.0, ((0, 8), (1, 32)), jnp.float32),
        "moment_expand": normal_values(seeds[12], (D, FF), 0.5, 6.0, ((0, 32),), jnp.float32),
        "weight_expand": normal_values(seeds[13], (D, FF), D ** -0.5, 0.1875, ((0, 32),), jnp.float32),
        "factor_expand": normal_values(seeds[14], (RANK, FF), 1.0, 6.0, (), jnp.float32),
        "grad_shrink": draw_grad_shrink(jax.random.fold_in(seeds[23], 71), 0),
        "error_shrink": normal_values(seeds[16], (REPS, FF, D), 0.5, 6.0, ((0, 8), (1, 32)), jnp.float32),
        "moment_shrink": normal_values(seeds[17], (FF, D), 0.5, 6.0, ((0, 32),), jnp.float32),
        "weight_shrink": normal_values(seeds[18], (FF, D), FF ** -0.5, 0.09375, ((0, 32),), jnp.float32),
        "factor_shrink": normal_values(seeds[19], (RANK, D), 1.0, 6.0, (), jnp.float32),
        "vector_grad": normal_values(seeds[20], (REPS, VEC), 1.0, 6.0, ((0, 8), (1, 32))),
        "vector_moment": normal_values(seeds[21], (VEC,), 0.5, 6.0, ((0, 32),), jnp.float32),
        "vector_weight": normal_values(seeds[22], (VEC,), 0.1, 1.5, ((0, 32),), jnp.float32),
    }


HIGHEST_PRECISION = lax.Precision.HIGHEST
momentum_decay = 0.9
learn_rate = 0.1

def compress_one(gradient, carried, moment, weight, factor):
    corrected = gradient.astype(jnp.float32) + carried
    basis = None
    for sweep in range(ROUNDS):
        row_factor = jnp.einsum('rn,amn->rm', factor, corrected, precision=HIGHEST_PRECISION)
        gram_matrix = jnp.dot(row_factor, row_factor.T, precision=HIGHEST_PRECISION)
        cholesky_factor = jnp.linalg.cholesky(gram_matrix)
        basis = jax.scipy.linalg.solve_triangular(cholesky_factor, row_factor, lower=True)
        factor = jnp.einsum('rm,amn->rn', basis, corrected, precision=HIGHEST_PRECISION) / REPS
    approx = jnp.dot(basis.T, factor, precision=HIGHEST_PRECISION)
    errors = corrected - approx[None]
    moments = momentum_decay * moment + approx
    weights = weight - learn_rate * moments
    return (errors, moments, weights, factor)

def reference(grad_joined, error_joined, moment_joined, weight_joined, factor_joined, grad_dense, error_dense, moment_dense, weight_dense, factor_dense, grad_expand, error_expand, moment_expand, weight_expand, factor_expand, grad_shrink, error_shrink, moment_shrink, weight_shrink, factor_shrink, vector_grad, vector_moment, vector_weight):
    first = compress_one(grad_joined, error_joined, moment_joined, weight_joined, factor_joined)
    second = compress_one(grad_dense, error_dense, moment_dense, weight_dense, factor_dense)
    third = compress_one(grad_expand, error_expand, moment_expand, weight_expand, factor_expand)
    fourth = compress_one(grad_shrink, error_shrink, moment_shrink, weight_shrink, factor_shrink)
    vector_mean = jnp.sum(vector_grad.astype(jnp.float32), axis=0) / REPS
    vector_moments = momentum_decay * vector_moment + vector_mean
    vector_weights = vector_weight - learn_rate * vector_moments
    return (first[0], first[1], first[2], first[3], second[0], second[1], second[2], second[3], third[0], third[1], third[2], third[3], fourth[0], fourth[1], fourth[2], fourth[3], vector_moments, vector_weights)
```

```python
import jax
import jax.numpy as jnp
from jax import lax
from jax.sharding import PartitionSpec as P

ROUNDS = 2


HIGHEST_PRECISION = lax.Precision.HIGHEST
momentum_decay = 0.9
learn_rate = 0.1


def row_product(factor, matrix):
    return lax.dot_general(
        factor,
        matrix,
        (((1,), (1,)), ((), ())),
        precision=HIGHEST_PRECISION,
        preferred_element_type=jnp.float32,
    )


def gram_of(row_factor):
    return lax.dot_general(
        row_factor,
        row_factor,
        (((1,), (1,)), ((), ())),
        precision=HIGHEST_PRECISION,
        preferred_element_type=jnp.float32,
    )


def mat(a, b):
    return jnp.dot(a, b, precision=HIGHEST_PRECISION, preferred_element_type=jnp.float32)


def inverse_cholesky(grams):
    lower = jnp.linalg.cholesky(grams)
    eye = jnp.broadcast_to(jnp.eye(grams.shape[-1], dtype=grams.dtype), grams.shape)
    return lax.linalg.triangular_solve(lower, eye, left_side=True, lower=True)


def shards(
    grad_joined,
    error_joined,
    moment_joined,
    weight_joined,
    factor_joined,
    grad_dense,
    error_dense,
    moment_dense,
    weight_dense,
    factor_dense,
    grad_expand,
    error_expand,
    moment_expand,
    weight_expand,
    factor_expand,
    grad_shrink,
    error_shrink,
    moment_shrink,
    weight_shrink,
    factor_shrink,
    vector_grad,
    vector_moment,
    vector_weight,
):
    replicas = lax.axis_size("rep")
    first_replica = lax.axis_index("rep") == 0
    gradients = [grad_joined, grad_dense, grad_expand, grad_shrink]
    carried = [error_joined, error_dense, error_expand, error_shrink]
    moment_list = [moment_joined, moment_dense, moment_expand, moment_shrink]
    weight_list = [weight_joined, weight_dense, weight_expand, weight_shrink]
    factors = [factor_joined, factor_dense, factor_expand, factor_shrink]
    members = range(4)
    corrected = [gradients[m][0].astype(jnp.float32) + carried[m][0] for m in members]
    vector_local = vector_grad[0].astype(jnp.float32)
    vector_total = None
    basis_list = []
    for sweep in range(ROUNDS):
        projected = [row_product(factors[m], corrected[m]) for m in members]
        if sweep == 0:
            summed = lax.psum((*projected, vector_local), "rep")
            vector_total = summed[4]
        else:
            summed = lax.psum(tuple(projected), "rep")
        grams = [
            jnp.where(first_replica, gram_of(summed[m]), jnp.zeros((), jnp.float32))
            for m in members
        ]
        partials = [mat(summed[m], corrected[m]) for m in members]
        packed = lax.psum(jnp.concatenate(partials + grams, axis=1), ("rep", "shard"))
        widths = [p.shape[1] for p in partials] + [g.shape[1] for g in grams]
        offsets = [sum(widths[:i]) for i in range(len(widths))]
        pieces = [packed[:, o : o + w] for o, w in zip(offsets, widths)]
        inverse = inverse_cholesky(jnp.stack(pieces[4:]))
        factors = [mat(inverse[m], pieces[m]) / replicas for m in members]
        basis_list = [mat(inverse[m], summed[m]) for m in members]
    results = []
    for m in members:
        approx = lax.dot_general(
            basis_list[m],
            factors[m],
            (((0,), (0,)), ((), ())),
            precision=HIGHEST_PRECISION,
            preferred_element_type=jnp.float32,
        )
        errors = (corrected[m] - approx)[None]
        moments = momentum_decay * moment_list[m] + approx
        weights = weight_list[m] - learn_rate * moments
        results.extend([errors, moments, weights, factors[m]])
    vector_moments = momentum_decay * vector_moment + vector_total / replicas
    vector_weights = vector_weight - learn_rate * vector_moments
    results.extend([vector_moments, vector_weights])
    return tuple(results)


def solution(mesh):
    big = P("rep", "shard", None)
    rows = P("shard", None)
    member_in = (big, big, rows, rows, P())
    member_out = (big, rows, rows, P())
    return jax.shard_map(
        shards,
        mesh=mesh,
        in_specs=member_in * 4 + (P("rep", "shard"), P("shard"), P("shard")),
        out_specs=member_out * 4 + (P("shard"), P("shard")),
        check_vma=False,
    )
```

```python
import jax
import jax.numpy as jnp
from jax import lax
from jax.sharding import PartitionSpec as P

ROUNDS = 2


HIGHEST_PRECISION = lax.Precision.HIGHEST
momentum_decay = 0.9
learn_rate = 0.1


def row_product(factor, matrix):
    return lax.dot_general(
        factor,
        matrix,
        (((1,), (1,)), ((), ())),
        precision=HIGHEST_PRECISION,
        preferred_element_type=jnp.float32,
    )


def gram_of(row_factor):
    return lax.dot_general(
        row_factor,
        row_factor,
        (((1,), (1,)), ((), ())),
        precision=HIGHEST_PRECISION,
        preferred_element_type=jnp.float32,
    )


def mat(a, b):
    return jnp.dot(a, b, precision=HIGHEST_PRECISION, preferred_element_type=jnp.float32)


def inverse_cholesky(grams):
    lower = jnp.linalg.cholesky(grams)
    eye = jnp.broadcast_to(jnp.eye(grams.shape[-1], dtype=grams.dtype), grams.shape)
    return lax.linalg.triangular_solve(lower, eye, left_side=True, lower=True)


def exchange(x, axis, size, bit):
    return lax.ppermute(x, axis, [(s, s ^ (1 << bit)) for s in range(size)])


def doubling_sum(values, axis):
    size = lax.axis_size(axis)
    for bit in range(size.bit_length() - 1):
        values = tuple(v + exchange(v, axis, size, bit) for v in values)
    return values


def halving_steps(sizes):
    shard_bits = sizes["shard"].bit_length() - 1
    rep_bits = sizes["rep"].bit_length() - 1
    preferred = [("shard", 0), ("shard", 1), ("shard", 3), ("rep", 0),
                 ("shard", 2), ("shard", 4), ("rep", 1), ("rep", 2)]
    steps = [(a, b) for a, b in preferred if b < (shard_bits if a == "shard" else rep_bits)]
    steps += [("shard", b) for b in range(shard_bits) if ("shard", b) not in steps]
    steps += [("rep", b) for b in range(rep_bits) if ("rep", b) not in steps]
    return steps


def halving_sum(x, sizes):
    steps = halving_steps(sizes)
    parts = 1 << len(steps)
    rows = x.shape[0]
    padded = -(-rows // (parts * 8)) * (parts * 8)
    block = jnp.pad(x, ((0, padded - rows), (0, 0)))
    for axis, bit in steps:
        upper = ((lax.axis_index(axis) >> bit) & 1) == 1
        half = block.shape[0] // 2
        low, high = block[:half], block[half:]
        keep = jnp.where(upper, high, low)
        give = jnp.where(upper, low, high)
        block = keep + exchange(give, axis, sizes[axis], bit)
    for axis, bit in reversed(steps):
        upper = ((lax.axis_index(axis) >> bit) & 1) == 1
        other = exchange(block, axis, sizes[axis], bit)
        block = jnp.where(
            upper, jnp.concatenate([other, block]), jnp.concatenate([block, other])
        )
    return block[:rows]


def shards(
    grad_joined,
    error_joined,
    moment_joined,
    weight_joined,
    factor_joined,
    grad_dense,
    error_dense,
    moment_dense,
    weight_dense,
    factor_dense,
    grad_expand,
    error_expand,
    moment_expand,
    weight_expand,
    factor_expand,
    grad_shrink,
    error_shrink,
    moment_shrink,
    weight_shrink,
    factor_shrink,
    vector_grad,
    vector_moment,
    vector_weight,
):
    replicas = lax.axis_size("rep")
    sizes = {"shard": lax.axis_size("shard"), "rep": replicas}
    first_replica = lax.axis_index("rep") == 0
    gradients = [grad_joined, grad_dense, grad_expand, grad_shrink]
    carried = [error_joined, error_dense, error_expand, error_shrink]
    moment_list = [moment_joined, moment_dense, moment_expand, moment_shrink]
    weight_list = [weight_joined, weight_dense, weight_expand, weight_shrink]
    factors = [factor_joined, factor_dense, factor_expand, factor_shrink]
    members = range(4)
    corrected = [gradients[m][0].astype(jnp.float32) + carried[m][0] for m in members]
    vector_local = vector_grad[0].astype(jnp.float32)
    vector_total = None
    basis_list = []
    for sweep in range(ROUNDS):
        projected = [row_product(factors[m], corrected[m]) for m in members]
        if sweep == 0:
            summed = doubling_sum((*projected, vector_local), "rep")
            vector_total = summed[4]
        else:
            summed = doubling_sum(tuple(projected), "rep")
        grams = [
            jnp.where(first_replica, gram_of(summed[m]), jnp.zeros((), jnp.float32))
            for m in members
        ]
        partials = [mat(summed[m], corrected[m]) for m in members]
        local = jnp.concatenate([p.reshape(-1) for p in partials + grams])
        packed = halving_sum(local.reshape(-1, 128), sizes).reshape(-1)
        shapes = [p.shape for p in partials + grams]
        offsets = [0]
        for shape in shapes:
            offsets.append(offsets[-1] + shape[0] * shape[1])
        pieces = [packed[o : o + a * b].reshape(a, b) for o, (a, b) in zip(offsets, shapes)]
        inverse = inverse_cholesky(jnp.stack(pieces[4:]))
        factors = [mat(inverse[m], pieces[m]) / replicas for m in members]
        basis_list = [mat(inverse[m], summed[m]) for m in members]
    results = []
    for m in members:
        approx = lax.dot_general(
            basis_list[m],
            factors[m],
            (((0,), (0,)), ((), ())),
            precision=HIGHEST_PRECISION,
            preferred_element_type=jnp.float32,
        )
        errors = (corrected[m] - approx)[None]
        moments = momentum_decay * moment_list[m] + approx
        weights = weight_list[m] - learn_rate * moments
        results.extend([errors, moments, weights, factors[m]])
    vector_moments = momentum_decay * vector_moment + vector_total / replicas
    vector_weights = vector_weight - learn_rate * vector_moments
    results.extend([vector_moments, vector_weights])
    return tuple(results)


def solution(mesh):
    big = P("rep", "shard", None)
    rows = P("shard", None)
    member_in = (big, big, rows, rows, P())
    member_out = (big, rows, rows, P())
    return jax.shard_map(
        shards,
        mesh=mesh,
        in_specs=member_in * 4 + (P("rep", "shard"), P("shard"), P("shard")),
        out_specs=member_out * 4 + (P("shard"), P("shard")),
        check_vma=False,
    )
```

```python
import jax
import jax.numpy as jnp
from jax import lax
from jax.sharding import PartitionSpec as P

ROUNDS = 2


HIGHEST_PRECISION = lax.Precision.HIGHEST
momentum_decay = 0.9
learn_rate = 0.1


def row_product(factor, matrix):
    return lax.dot_general(
        factor,
        matrix,
        (((1,), (1,)), ((), ())),
        precision=HIGHEST_PRECISION,
        preferred_element_type=jnp.float32,
    )


def gram_of(row_factor):
    return lax.dot_general(
        row_factor,
        row_factor,
        (((1,), (1,)), ((), ())),
        precision=HIGHEST_PRECISION,
        preferred_element_type=jnp.float32,
    )


def mat(a, b):
    return jnp.dot(a, b, precision=HIGHEST_PRECISION, preferred_element_type=jnp.float32)


def inverse_cholesky(grams):
    lower = jnp.linalg.cholesky(grams)
    eye = jnp.broadcast_to(jnp.eye(grams.shape[-1], dtype=grams.dtype), grams.shape)
    return lax.linalg.triangular_solve(lower, eye, left_side=True, lower=True)


def exchange(x, axis, size, bit):
    return lax.ppermute(x, axis, [(s, s ^ (1 << bit)) for s in range(size)])


def doubling_sum(values, axis):
    size = lax.axis_size(axis)
    flat = jnp.concatenate([v.reshape(-1) for v in values])
    count = flat.shape[0]
    padded = -(-count // 1024) * 1024
    block = jnp.pad(flat, (0, padded - count)).reshape(-1, 128)
    for bit in range(size.bit_length() - 1):
        block = block + exchange(block, axis, size, bit)
    flat = block.reshape(-1)
    out, start = [], 0
    for v in values:
        out.append(flat[start : start + v.size].reshape(v.shape))
        start += v.size
    return tuple(out)


def halving_steps(sizes):
    shard_bits = sizes["shard"].bit_length() - 1
    rep_bits = sizes["rep"].bit_length() - 1
    preferred = [("shard", 0), ("shard", 1), ("shard", 3), ("rep", 0),
                 ("shard", 2), ("shard", 4), ("rep", 1), ("rep", 2)]
    steps = [(a, b) for a, b in preferred if b < (shard_bits if a == "shard" else rep_bits)]
    steps += [("shard", b) for b in range(shard_bits) if ("shard", b) not in steps]
    steps += [("rep", b) for b in range(rep_bits) if ("rep", b) not in steps]
    return steps


def halving_sum(x, sizes):
    steps = halving_steps(sizes)
    parts = 1 << len(steps)
    rows = x.shape[0]
    padded = -(-rows // (parts * 8)) * (parts * 8)
    block = jnp.pad(x, ((0, padded - rows), (0, 0)))
    for axis, bit in steps:
        upper = ((lax.axis_index(axis) >> bit) & 1) == 1
        half = block.shape[0] // 2
        low, high = block[:half], block[half:]
        keep = jnp.where(upper, high, low)
        give = jnp.where(upper, low, high)
        block = keep + exchange(give, axis, sizes[axis], bit)
    for axis, bit in reversed(steps):
        upper = ((lax.axis_index(axis) >> bit) & 1) == 1
        other = exchange(block, axis, sizes[axis], bit)
        block = jnp.where(
            upper, jnp.concatenate([other, block]), jnp.concatenate([block, other])
        )
    return block[:rows]


def shards(
    grad_joined,
    error_joined,
    moment_joined,
    weight_joined,
    factor_joined,
    grad_dense,
    error_dense,
    moment_dense,
    weight_dense,
    factor_dense,
    grad_expand,
    error_expand,
    moment_expand,
    weight_expand,
    factor_expand,
    grad_shrink,
    error_shrink,
    moment_shrink,
    weight_shrink,
    factor_shrink,
    vector_grad,
    vector_moment,
    vector_weight,
):
    replicas = lax.axis_size("rep")
    sizes = {"shard": lax.axis_size("shard"), "rep": replicas}
    first_replica = lax.axis_index("rep") == 0
    gradients = [grad_joined, grad_dense, grad_expand, grad_shrink]
    carried = [error_joined, error_dense, error_expand, error_shrink]
    moment_list = [moment_joined, moment_dense, moment_expand, moment_shrink]
    weight_list = [weight_joined, weight_dense, weight_expand, weight_shrink]
    factors = [factor_joined, factor_dense, factor_expand, factor_shrink]
    members = range(4)
    corrected = [gradients[m][0].astype(jnp.float32) + carried[m][0] for m in members]
    vector_local = vector_grad[0].astype(jnp.float32)
    vector_total = None
    basis_list = []
    for sweep in range(ROUNDS):
        projected = [row_product(factors[m], corrected[m]) for m in members]
        if sweep == 0:
            summed = doubling_sum((*projected, vector_local), "rep")
            vector_total = summed[4]
        else:
            summed = doubling_sum(tuple(projected), "rep")
        grams = [
            jnp.where(first_replica, gram_of(summed[m]), jnp.zeros((), jnp.float32))
            for m in members
        ]
        partials = [mat(summed[m], corrected[m]) for m in members]
        local = jnp.concatenate([p.reshape(-1) for p in partials + grams])
        packed = halving_sum(local.reshape(-1, 128), sizes).reshape(-1)
        shapes = [p.shape for p in partials + grams]
        offsets = [0]
        for shape in shapes:
            offsets.append(offsets[-1] + shape[0] * shape[1])
        pieces = [packed[o : o + a * b].reshape(a, b) for o, (a, b) in zip(offsets, shapes)]
        inverse = inverse_cholesky(jnp.stack(pieces[4:]))
        factors = [mat(inverse[m], pieces[m]) / replicas for m in members]
        basis_list = [mat(inverse[m], summed[m]) for m in members]
    results = []
    for m in members:
        approx = lax.dot_general(
            basis_list[m],
            factors[m],
            (((0,), (0,)), ((), ())),
            precision=HIGHEST_PRECISION,
            preferred_element_type=jnp.float32,
        )
        errors = (corrected[m] - approx)[None]
        moments = momentum_decay * moment_list[m] + approx
        weights = weight_list[m] - learn_rate * moments
        results.extend([errors, moments, weights, factors[m]])
    vector_moments = momentum_decay * vector_moment + vector_total / replicas
    vector_weights = vector_weight - learn_rate * vector_moments
    results.extend([vector_moments, vector_weights])
    return tuple(results)


def solution(mesh):
    big = P("rep", "shard", None)
    rows = P("shard", None)
    member_in = (big, big, rows, rows, P())
    member_out = (big, rows, rows, P())
    return jax.shard_map(
        shards,
        mesh=mesh,
        in_specs=member_in * 4 + (P("rep", "shard"), P("shard"), P("shard")),
        out_specs=member_out * 4 + (P("shard"), P("shard")),
        check_vma=False,
    )
```

```python
import jax
import jax.numpy as jnp
from jax import lax
from jax.sharding import PartitionSpec as P

ROUNDS = 2


HIGHEST_PRECISION = lax.Precision.HIGHEST
momentum_decay = 0.9
learn_rate = 0.1


def row_product(factor, matrix):
    return lax.dot_general(
        factor,
        matrix,
        (((1,), (1,)), ((), ())),
        precision=HIGHEST_PRECISION,
        preferred_element_type=jnp.float32,
    )


def gram_of(row_factor):
    return lax.dot_general(
        row_factor,
        row_factor,
        (((1,), (1,)), ((), ())),
        precision=HIGHEST_PRECISION,
        preferred_element_type=jnp.float32,
    )


def mat(a, b):
    return jnp.dot(a, b, precision=HIGHEST_PRECISION, preferred_element_type=jnp.float32)


def inverse_cholesky(grams):
    lower = jnp.linalg.cholesky(grams)
    eye = jnp.broadcast_to(jnp.eye(grams.shape[-1], dtype=grams.dtype), grams.shape)
    return lax.linalg.triangular_solve(lower, eye, left_side=True, lower=True)


def exchange(x, axis, size, bit):
    return lax.ppermute(x, axis, [(s, s ^ (1 << bit)) for s in range(size)])


def doubling_sum(values, axis):
    size = lax.axis_size(axis)
    flat = jnp.concatenate([v.reshape(-1) for v in values])
    count = flat.shape[0]
    padded = -(-count // 1024) * 1024
    block = jnp.pad(flat, (0, padded - count)).reshape(-1, 128)
    for bit in range(size.bit_length() - 1):
        block = block + exchange(block, axis, size, bit)
    flat = block.reshape(-1)
    out, start = [], 0
    for v in values:
        out.append(flat[start : start + v.size].reshape(v.shape))
        start += v.size
    return tuple(out)


def halving_steps(sizes):
    shard_bits = sizes["shard"].bit_length() - 1
    rep_bits = sizes["rep"].bit_length() - 1
    preferred = [("shard", 0), ("shard", 1), ("shard", 3), ("rep", 0),
                 ("shard", 2), ("shard", 4), ("rep", 1), ("rep", 2)]
    steps = [(a, b) for a, b in preferred if b < (shard_bits if a == "shard" else rep_bits)]
    steps += [("shard", b) for b in range(shard_bits) if ("shard", b) not in steps]
    steps += [("rep", b) for b in range(rep_bits) if ("rep", b) not in steps]
    return steps


def halving_sum(x, sizes, scatter_steps=4):
    steps = halving_steps(sizes)
    scatter, whole = steps[:scatter_steps], steps[scatter_steps:]
    parts = 1 << len(scatter)
    rows = x.shape[0]
    padded = -(-rows // (parts * 8)) * (parts * 8)
    block = jnp.pad(x, ((0, padded - rows), (0, 0)))
    for axis, bit in scatter:
        upper = ((lax.axis_index(axis) >> bit) & 1) == 1
        half = block.shape[0] // 2
        low, high = block[:half], block[half:]
        keep = jnp.where(upper, high, low)
        give = jnp.where(upper, low, high)
        block = keep + exchange(give, axis, sizes[axis], bit)
    for axis, bit in whole:
        block = block + exchange(block, axis, sizes[axis], bit)
    for axis, bit in reversed(scatter):
        upper = ((lax.axis_index(axis) >> bit) & 1) == 1
        other = exchange(block, axis, sizes[axis], bit)
        block = jnp.where(
            upper, jnp.concatenate([other, block]), jnp.concatenate([block, other])
        )
    return block[:rows]


def shards(
    grad_joined,
    error_joined,
    moment_joined,
    weight_joined,
    factor_joined,
    grad_dense,
    error_dense,
    moment_dense,
    weight_dense,
    factor_dense,
    grad_expand,
    error_expand,
    moment_expand,
    weight_expand,
    factor_expand,
    grad_shrink,
    error_shrink,
    moment_shrink,
    weight_shrink,
    factor_shrink,
    vector_grad,
    vector_moment,
    vector_weight,
):
    replicas = lax.axis_size("rep")
    sizes = {"shard": lax.axis_size("shard"), "rep": replicas}
    first_replica = lax.axis_index("rep") == 0
    gradients = [grad_joined, grad_dense, grad_expand, grad_shrink]
    carried = [error_joined, error_dense, error_expand, error_shrink]
    moment_list = [moment_joined, moment_dense, moment_expand, moment_shrink]
    weight_list = [weight_joined, weight_dense, weight_expand, weight_shrink]
    factors = [factor_joined, factor_dense, factor_expand, factor_shrink]
    members = range(4)
    corrected = [gradients[m][0].astype(jnp.float32) + carried[m][0] for m in members]
    vector_local = vector_grad[0].astype(jnp.float32)
    vector_total = None
    basis_list = []
    for sweep in range(ROUNDS):
        projected = [row_product(factors[m], corrected[m]) for m in members]
        if sweep == 0:
            summed = doubling_sum((*projected, vector_local), "rep")
            vector_total = summed[4]
        else:
            summed = doubling_sum(tuple(projected), "rep")
        grams = [
            jnp.where(first_replica, gram_of(summed[m]), jnp.zeros((), jnp.float32))
            for m in members
        ]
        partials = [mat(summed[m], corrected[m]) for m in members]
        local = jnp.concatenate([p.reshape(-1) for p in partials + grams])
        packed = halving_sum(local.reshape(-1, 128), sizes).reshape(-1)
        shapes = [p.shape for p in partials + grams]
        offsets = [0]
        for shape in shapes:
            offsets.append(offsets[-1] + shape[0] * shape[1])
        pieces = [packed[o : o + a * b].reshape(a, b) for o, (a, b) in zip(offsets, shapes)]
        inverse = inverse_cholesky(jnp.stack(pieces[4:]))
        factors = [mat(inverse[m], pieces[m]) / replicas for m in members]
        basis_list = [mat(inverse[m], summed[m]) for m in members]
    results = []
    for m in members:
        approx = lax.dot_general(
            basis_list[m],
            factors[m],
            (((0,), (0,)), ((), ())),
            precision=HIGHEST_PRECISION,
            preferred_element_type=jnp.float32,
        )
        errors = (corrected[m] - approx)[None]
        moments = momentum_decay * moment_list[m] + approx
        weights = weight_list[m] - learn_rate * moments
        results.extend([errors, moments, weights, factors[m]])
    vector_moments = momentum_decay * vector_moment + vector_total / replicas
    vector_weights = vector_weight - learn_rate * vector_moments
    results.extend([vector_moments, vector_weights])
    return tuple(results)


def solution(mesh):
    big = P("rep", "shard", None)
    rows = P("shard", None)
    member_in = (big, big, rows, rows, P())
    member_out = (big, rows, rows, P())
    return jax.shard_map(
        shards,
        mesh=mesh,
        in_specs=member_in * 4 + (P("rep", "shard"), P("shard"), P("shard")),
        out_specs=member_out * 4 + (P("shard"), P("shard")),
        check_vma=False,
    )
```

```python
import jax
import jax.numpy as jnp
from jax import lax
from jax.sharding import PartitionSpec as P

ROUNDS = 2


HIGHEST_PRECISION = lax.Precision.HIGHEST
momentum_decay = 0.9
learn_rate = 0.1


def row_product(factor, matrix):
    return lax.dot_general(
        factor,
        matrix,
        (((1,), (1,)), ((), ())),
        precision=HIGHEST_PRECISION,
        preferred_element_type=jnp.float32,
    )


def gram_of(row_factor):
    return lax.dot_general(
        row_factor,
        row_factor,
        (((1,), (1,)), ((), ())),
        precision=HIGHEST_PRECISION,
        preferred_element_type=jnp.float32,
    )


def mat(a, b):
    return jnp.dot(a, b, precision=HIGHEST_PRECISION, preferred_element_type=jnp.float32)


def inverse_cholesky(grams):
    lower = jnp.linalg.cholesky(grams)
    eye = jnp.broadcast_to(jnp.eye(grams.shape[-1], dtype=grams.dtype), grams.shape)
    return lax.linalg.triangular_solve(lower, eye, left_side=True, lower=True)


def exchange(x, axis, size, bit):
    return lax.ppermute(x, axis, [(s, s ^ (1 << bit)) for s in range(size)])


def doubling_sum(values, axis):
    size = lax.axis_size(axis)
    flat = jnp.concatenate([v.reshape(-1) for v in values])
    count = flat.shape[0]
    padded = -(-count // 1024) * 1024
    block = jnp.pad(flat, (0, padded - count)).reshape(-1, 128)
    for bit in range(size.bit_length() - 1):
        block = block + exchange(block, axis, size, bit)
    flat = block.reshape(-1)
    out, start = [], 0
    for v in values:
        out.append(flat[start : start + v.size].reshape(v.shape))
        start += v.size
    return tuple(out)


def halving_steps(sizes):
    shard_bits = sizes["shard"].bit_length() - 1
    rep_bits = sizes["rep"].bit_length() - 1
    preferred = [("shard", 0), ("shard", 1), ("shard", 3), ("rep", 0),
                 ("shard", 2), ("shard", 4), ("rep", 1), ("rep", 2)]
    steps = [(a, b) for a, b in preferred if b < (shard_bits if a == "shard" else rep_bits)]
    steps += [("shard", b) for b in range(shard_bits) if ("shard", b) not in steps]
    steps += [("rep", b) for b in range(rep_bits) if ("rep", b) not in steps]
    return steps


def halving_sum(x, sizes, scatter_steps=3):
    steps = halving_steps(sizes)
    scatter, whole = steps[:scatter_steps], steps[scatter_steps:]
    parts = 1 << len(scatter)
    rows = x.shape[0]
    padded = -(-rows // (parts * 8)) * (parts * 8)
    block = jnp.pad(x, ((0, padded - rows), (0, 0)))
    for axis, bit in scatter:
        upper = ((lax.axis_index(axis) >> bit) & 1) == 1
        half = block.shape[0] // 2
        low, high = block[:half], block[half:]
        keep = jnp.where(upper, high, low)
        give = jnp.where(upper, low, high)
        block = keep + exchange(give, axis, sizes[axis], bit)
    for axis, bit in whole:
        block = block + exchange(block, axis, sizes[axis], bit)
    for axis, bit in reversed(scatter):
        upper = ((lax.axis_index(axis) >> bit) & 1) == 1
        other = exchange(block, axis, sizes[axis], bit)
        block = jnp.where(
            upper, jnp.concatenate([other, block]), jnp.concatenate([block, other])
        )
    return block[:rows]


def step(
    grad_joined,
    error_joined,
    moment_joined,
    weight_joined,
    factor_joined,
    grad_dense,
    error_dense,
    moment_dense,
    weight_dense,
    factor_dense,
    grad_expand,
    error_expand,
    moment_expand,
    weight_expand,
    factor_expand,
    grad_shrink,
    error_shrink,
    moment_shrink,
    weight_shrink,
    factor_shrink,
    vector_grad,
    vector_moment,
    vector_weight,
):
    replicas = lax.axis_size("rep")
    sizes = {"shard": lax.axis_size("shard"), "rep": replicas}
    first_replica = lax.axis_index("rep") == 0
    gradients = [grad_joined, grad_dense, grad_expand, grad_shrink]
    carried = [error_joined, error_dense, error_expand, error_shrink]
    moment_list = [moment_joined, moment_dense, moment_expand, moment_shrink]
    weight_list = [weight_joined, weight_dense, weight_expand, weight_shrink]
    factors = [factor_joined, factor_dense, factor_expand, factor_shrink]
    members = range(4)
    corrected = [gradients[m][0].astype(jnp.float32) + carried[m][0] for m in members]
    vector_local = vector_grad[0].astype(jnp.float32)
    vector_total = None
    basis_list = []
    for sweep in range(ROUNDS):
        if sweep == 0:
            projected = [row_product(factors[m], corrected[m]) for m in members]
            summed = doubling_sum((*projected, vector_local), "rep")
            vector_total = summed[4]
        else:
            raw = [row_product(pieces[m], corrected[m]) for m in members]
            raw_sum = doubling_sum(tuple(raw), "rep")
            summed = [mat(inverse[m], raw_sum[m]) / replicas for m in members]
        grams = [
            jnp.where(first_replica, gram_of(summed[m]), jnp.zeros((), jnp.float32))
            for m in members
        ]
        partials = [mat(summed[m], corrected[m]) for m in members]
        local = jnp.concatenate([p.reshape(-1) for p in partials + grams])
        packed = halving_sum(local.reshape(-1, 128), sizes).reshape(-1)
        shapes = [p.shape for p in partials + grams]
        offsets = [0]
        for shape in shapes:
            offsets.append(offsets[-1] + shape[0] * shape[1])
        pieces = [packed[o : o + a * b].reshape(a, b) for o, (a, b) in zip(offsets, shapes)]
        inverse = inverse_cholesky(jnp.stack(pieces[4:]))
        factors = [mat(inverse[m], pieces[m]) / replicas for m in members]
        basis_list = [mat(inverse[m], summed[m]) for m in members]
    results = []
    for m in members:
        approx = lax.dot_general(
            basis_list[m],
            factors[m],
            (((0,), (0,)), ((), ())),
            precision=HIGHEST_PRECISION,
            preferred_element_type=jnp.float32,
        )
        errors = (corrected[m] - approx)[None]
        moments = momentum_decay * moment_list[m] + approx
        weights = weight_list[m] - learn_rate * moments
        results.extend([errors, moments, weights, factors[m]])
    vector_moments = momentum_decay * vector_moment + vector_total / replicas
    vector_weights = vector_weight - learn_rate * vector_moments
    results.extend([vector_moments, vector_weights])
    return tuple(results)


def solution(mesh):
    big = P("rep", "shard", None)
    rows = P("shard", None)
    member_in = (big, big, rows, rows, P())
    member_out = (big, rows, rows, P())
    return jax.shard_map(
        step,
        mesh=mesh,
        in_specs=member_in * 4 + (P("rep", "shard"), P("shard"), P("shard")),
        out_specs=member_out * 4 + (P("shard"), P("shard")),
        check_vma=False,
    )
```
